512 devices in a mesh: req: 128 (over z, y, core), grp: 4 (over x).
Axes of the slice: x: 4, y: 8, z: 8, core: 2. Of those that a mesh axis runs over, the one named last changes fastest.
Arguments:
- owner_slab: bfloat16 [65536, 1024], P('req'), may hold values from -6 to 6
- segment_ids: int32 [128, 512], P('req'), may hold values from 0 to 511, as said below
- head_weights: bfloat16 [1024, 16, 192], P(None, 'grp')
- merge_weights: bfloat16 [16, 64, 1024], P('grp'), may hold values from -0.1875 to 0.1875
- first_gain: float32 [1024], replicated, may hold values from 0.25 to 1.75
- first_bias: float32 [1024], replicated, may hold values from -3 to 3
- up_weights: bfloat16 [1024, 4096], P('req', 'grp'), may hold values from -0.1875 to 0.1875
- down_weights: bfloat16 [4096, 1024], P('grp', 'req'), may hold values from -0.09375 to 0.09375
- second_gain: float32 [1024], replicated, may hold values from 0.25 to 1.75
- second_bias: float32 [1024], replicated, may hold values from -3 to 3
- page_table: int32 [128, 4], P('req'), may hold values from 0 to 3, each once within a row
- row_map: int32 [128, 4, 128], P('req', 'grp'), may hold values from 0 to 127, each once within a row
Outputs:
- layer_out: bfloat16 [65536, 1024], P(('req', 'grp'))
- cache_pages: bfloat16 [512, 128, 16, 128], P('req', None, 'grp')
The draws below stay inside these ranges and needn't reach their ends.
Inputs may be any that keep to these rules, and one draw needn't show every extreme that they name: `segment_ids`: within each slab the ids start at 0, never fall and rise by at most one from row to row; in one slab all 512 rows form a single request, and in one other slab every row is a request of its own.
All inputs are finite; a program needn't handle non-finite values.
Results may differ from the reference program's by a relative error of at most 0.0075.
Values may be sent and summed in bfloat16 or wider, within the bound.
No kernel may reach another device: no remote copies, remote signals or barrier semaphores. Data moves between devices by JAX's collectives and lax.ppermute only.
A program may use at most 64 MiB of HBM per device.

```python
import math
from functools import partial
import jax
import jax.numpy as jnp
from jax import lax

D = 1024
HEADS = 16
HDIM = 64
FF = 4096
PAGE = 128
CAP = 512
SLAB_PAGES = 4
ROWS_Q = 128
SLOT = 1
TOKENS = 65536
N_REQ = 128
N_GRP = 4


def draw_segment_ids(key, part):
    rates = jax.random.randint(jax.random.fold_in(key, 11), (N_REQ, 1), 8, 97)
    coins = jax.random.randint(jax.random.fold_in(key, 12), (N_REQ, CAP), 0, 1 << 20)
    position = jnp.arange(CAP, dtype=jnp.int32)[None, :]
    cuts = (coins % rates == 0) & (position > 0)
    longest = jax.random.randint(jax.random.fold_in(key, 13), (), 0, N_REQ)
    single = (longest + 1) % N_REQ
    owners = jnp.arange(N_REQ, dtype=jnp.int32)[:, None]
    cuts = (cuts | (owners == single) & (position > 0)) & (owners != longest)
    return jnp.cumsum(cuts.astype(jnp.int32), axis=1).astype(jnp.int32)


def draw_head_weights(key, part):
    base = jax.random.normal(jax.random.fold_in(key, 21), (D, HEADS, 3 * HDIM), jnp.float32) / math.sqrt(D)
    return base.astype(jnp.bfloat16)


def block_scale(stream_key, shape, split, least, high):
    def one(dim, parts):
        heights = jax.random.uniform(jax.random.fold_in(jax.random.fold_in(stream_key, 6), dim), (parts,), jnp.float32, least / len(split), high / len(split))
        return jnp.repeat(jnp.exp(heights), shape[dim] // parts).reshape((-1,) + (1,) * (len(shape) - dim - 1))

    factor_of = one(*split[0])
    for cut in split[1:]:
        factor_of = factor_of * one(*cut)
    return factor_of


def gaussian(rng, dims, scale, limit, cuts=(), kind=jnp.bfloat16):
    loudness = block_scale(rng, dims, cuts, -0.22, 0.18) if cuts else 1.0
    values = jax.random.normal(rng, dims, jnp.float32) * scale * loudness
    return jnp.minimum(jnp.maximum(values, -limit), limit).astype(kind)


def setup_inputs(seed: int = 0) -> dict:
    streams_of = jax.random.split(jax.random.key(seed), 13)
    return {
        "owner_slab": gaussian(streams_of[0], (TOKENS, D), 1.0, 6.0, ((0, 128),)),
        "segment_ids": draw_segment_ids(jax.random.fold_in(streams_of[12], 71), 0),
        "head_weights": draw_head_weights(jax.random.fold_in(streams_of[12], 71), 0),
        "merge_weights": gaussian(streams_of[3], (HEADS, HDIM, D), (HEADS * HDIM) ** -0.5, 0.1875, ((0, 4),)),
        "first_gain": jnp.clip(1.0 + 0.15 * jax.random.normal(streams_of[4], (D,), jnp.float32), 0.25, 1.75),
        "first_bias": gaussian(streams_of[5], (D,), 0.5, 3.0, (), jnp.float32),
        "up_weights": gaussian(streams_of[6], (D, FF), D ** -0.5, 0.1875, ((0, 128), (1, 4))),
        "down_weights": gaussian(streams_of[7], (FF, D), FF ** -0.5, 0.09375, ((0, 4), (1, 128))),
        "second_gain": jnp.clip(1.0 + 0.15 * jax.random.normal(streams_of[8], (D,), jnp.float32), 0.25, 1.75),
        "second_bias": gaussian(streams_of[9], (D,), 0.5, 3.0, (), jnp.float32),
        "page_table": jax.vmap(lambda own: jax.random.permutation(own, SLAB_PAGES))(jax.random.split(streams_of[10], N_REQ)).reshape((N_REQ, SLAB_PAGES)).astype(jnp.int32),
        "row_map": jax.vmap(lambda own: jax.random.permutation(own, ROWS_Q))(jax.random.split(streams_of[11], N_REQ * N_GRP)).reshape((N_REQ, N_GRP, ROWS_Q)).astype(jnp.int32),
    }


EPSILON = 1e-05

def layer_norm(values, gain, bias):
    center = values - lax.optimization_barrier(jnp.mean(values, axis=-1, keepdims=True))
    spread = lax.optimization_barrier(jnp.mean(center * center, axis=-1, keepdims=True))
    return center * lax.rsqrt(spread + EPSILON) * gain + bias

def owner_block(operands, head_weights, merge_weights, first_gain, first_bias, up_weights, down_weights, second_gain, second_bias):
    rows, segment, pages = operands
    projected = jnp.einsum('nd,dhc->nhc', rows.astype(jnp.float32), head_weights.astype(jnp.float32)).astype(jnp.bfloat16)
    queries = projected[:, :, :HDIM].astype(jnp.float32)
    key_rows = projected[:, :, HDIM:2 * HDIM].astype(jnp.float32)
    value_rows = projected[:, :, 2 * HDIM:].astype(jnp.float32)
    position = jnp.arange(CAP, dtype=jnp.int32)
    allowed = (position[:, None] >= position[None, :]) & (segment[:, None] == segment[None, :])
    scores = jnp.einsum('qhd,khd->hqk', queries, key_rows) * (1.0 / HDIM ** 0.5)
    scores = jnp.where(allowed[None, :, :], scores, -1e+30)
    probs = jax.nn.softmax(scores, axis=-1).astype(jnp.bfloat16)
    attended = jnp.einsum('hqk,khd->qhd', probs.astype(jnp.float32), value_rows).astype(jnp.bfloat16)
    mixed = jnp.einsum('qhd,hde->qe', attended.astype(jnp.float32), merge_weights.astype(jnp.float32))
    hidden = layer_norm(rows.astype(jnp.float32) + mixed, first_gain, first_bias).astype(jnp.bfloat16)
    activated = jax.nn.gelu(jnp.dot(hidden, up_weights, preferred_element_type=jnp.float32), approximate=False).astype(jnp.bfloat16)
    lowered = jnp.dot(activated, down_weights, preferred_element_type=jnp.float32)
    finished = layer_norm(hidden.astype(jnp.float32) + lowered, second_gain, second_bias).astype(jnp.bfloat16)
    stacked = projected[:, :, HDIM:].reshape(SLAB_PAGES, PAGE, HEADS, 2 * HDIM)
    written = jnp.zeros_like(stacked).at[pages].set(stacked)
    return (finished, written)

def reference(owner_slab, segment_ids, head_weights, merge_weights, first_gain, first_bias, up_weights, down_weights, second_gain, second_bias, page_table, row_map):
    block = partial(owner_block, head_weights=head_weights, merge_weights=merge_weights, first_gain=first_gain, first_bias=first_bias, up_weights=up_weights, down_weights=down_weights, second_gain=second_gain, second_bias=second_bias)
    finished, written = lax.map(block, (owner_slab.reshape(N_REQ, CAP, D), segment_ids, page_table))
    owner = jnp.arange(N_REQ, dtype=jnp.int32)[:, None, None]
    quarter = jnp.arange(N_GRP, dtype=jnp.int32)[None, :, None]
    target = (row_map // SLOT * N_GRP + quarter) * ROWS_Q + owner * SLOT + row_map % SLOT
    layer_out = jnp.zeros((TOKENS, D), jnp.bfloat16).at[target.reshape(-1)].set(finished.reshape(TOKENS, D))
    cache_pages = written.reshape(N_REQ * SLAB_PAGES, PAGE, HEADS, 2 * HDIM)
    return (layer_out, cache_pages)
```

```python
import math

import jax
import jax.numpy as jnp
import numpy as np
from jax import lax
from jax.sharding import Mesh
from jax.sharding import PartitionSpec as P

EPSILON = 1e-05
REQ = ("rz", "ry", "rc")


def layer_norm(values, gain, bias):
    center = values - jnp.mean(values, axis=-1, keepdims=True)
    spread = jnp.mean(center * center, axis=-1, keepdims=True)
    return center * lax.rsqrt(spread + EPSILON) * gain + bias


def split_req(mesh):
    column = mesh.devices[:, 0]
    try:
        cores = len({d.core_on_chip for d in column})
        ys = len({d.coords[1] for d in column})
        zs = len({d.coords[2] for d in column})
    except AttributeError:
        return (column.shape[0], 1, 1)
    if zs * ys * cores != column.shape[0]:
        return (column.shape[0], 1, 1)
    return (zs, ys, cores)


def gather_rows(block, first, second):
    a = lax.all_gather(block, first, axis=0, tiled=False)
    b = lax.all_gather(a, second, axis=0, tiled=False)
    c = lax.all_gather(b, "rc", axis=0, tiled=False)
    if first == "ry":
        c = jnp.transpose(c, (1, 2, 0, 3, 4))
    else:
        c = jnp.transpose(c, (2, 1, 0, 3, 4))
    return c.reshape(-1, block.shape[1])


def local(
    owner_slab,
    segment_ids,
    head_weights,
    merge_weights,
    first_gain,
    first_bias,
    up_weights,
    down_weights,
    second_gain,
    second_bias,
    page_table,
    row_map,
):
    group = lax.axis_size("grp")
    owners = lax.axis_size(REQ)
    zs = lax.axis_size("rz")
    rows_all = owner_slab.shape[0]
    width = owner_slab.shape[1]
    quarter = rows_all // group
    local_heads = head_weights.shape[1]
    head_dim = head_weights.shape[2] // 3

    up_full = gather_rows(up_weights, "ry", "rz")
    down_full_t = gather_rows(jnp.transpose(down_weights), "rz", "ry")

    projected = jnp.einsum(
        "nd,dhc->nhc", owner_slab, head_weights, preferred_element_type=jnp.float32
    ).astype(jnp.bfloat16)
    queries = jnp.moveaxis(projected[:, :, :head_dim], 1, 0)
    key_rows = jnp.moveaxis(projected[:, :, head_dim : 2 * head_dim], 1, 0)
    value_rows = jnp.moveaxis(projected[:, :, 2 * head_dim :], 1, 0)
    segment = segment_ids[0]
    position = jnp.arange(rows_all, dtype=jnp.int32)
    allowed = (position[:, None] >= position[None, :]) & (segment[:, None] == segment[None, :])
    scale = 1.0 / math.sqrt(head_dim)

    def one_head(operands):
        query_head, key_head, value_head = operands
        scores = (
            lax.dot_general(
                query_head, key_head, (((1,), (1,)), ((), ())), preferred_element_type=jnp.float32
            )
            * scale
        )
        scores = jnp.where(allowed, scores, -1e30)
        probs = jax.nn.softmax(scores, axis=-1).astype(jnp.bfloat16)
        return jnp.dot(probs, value_head, preferred_element_type=jnp.float32).astype(jnp.bfloat16)

    attended = jnp.moveaxis(lax.map(one_head, (queries, key_rows, value_rows)), 0, 1)
    own = lax.axis_index("grp")
    own_rows = lax.dynamic_slice_in_dim(owner_slab, own * quarter, quarter, 0).astype(jnp.float32)
    partial_rows = jnp.einsum(
        "nhd,hde->ne", attended, merge_weights, preferred_element_type=jnp.float32
    )
    mixed = lax.psum_scatter(partial_rows, "grp", scatter_dimension=0, tiled=True)
    hidden = layer_norm(own_rows + mixed, first_gain, first_bias).astype(jnp.bfloat16)
    slots = quarter // owners
    placed = jnp.zeros_like(hidden).at[row_map[0, 0]].set(hidden)
    staged = placed.reshape(zs, owners // zs, slots * width)
    staged = lax.all_to_all(staged, "rz", split_axis=0, concat_axis=0, tiled=True)
    staged = lax.all_to_all(staged, ("ry", "rc"), split_axis=1, concat_axis=1, tiled=True)
    even_rows = staged.reshape(quarter, width)
    group_rows = lax.all_gather(even_rows, "grp", axis=0, tiled=True)
    raised = jnp.dot(group_rows, up_full, preferred_element_type=jnp.float32)
    activated = jax.nn.gelu(raised, approximate=False).astype(jnp.bfloat16)
    lowered_all = lax.dot_general(
        activated, down_full_t, (((1,), (1,)), ((), ())), preferred_element_type=jnp.float32
    )
    lowered = lax.psum_scatter(lowered_all, "grp", scatter_dimension=0, tiled=True)
    layer_out = layer_norm(
        even_rows.astype(jnp.float32) + lowered, second_gain, second_bias
    ).astype(jnp.bfloat16)
    page_count = page_table.shape[1]
    page_rows = rows_all // page_count
    stacked = projected[:, :, head_dim:].reshape(page_count, page_rows, local_heads, 2 * head_dim)
    cache_pages = jnp.zeros_like(stacked).at[page_table[0]].set(stacked)
    return (layer_out, cache_pages)


def solution(mesh):
    zs, ys, cores = split_req(mesh)
    devices = np.asarray(mesh.devices).reshape(zs, ys, cores, mesh.devices.shape[1])
    inner = Mesh(devices, REQ + ("grp",))
    in_specs = (
        P(REQ, None),
        P(REQ, None),
        P(None, "grp", None),
        P("grp", None, None),
        P(),
        P(),
        P(REQ, "grp"),
        P("grp", REQ),
        P(),
        P(),
        P(REQ, None),
        P(REQ, "grp", None),
    )
    out_specs = (P(REQ + ("grp",), None), P(REQ, None, "grp", None))
    return jax.shard_map(local, mesh=inner, in_specs=in_specs, out_specs=out_specs, check_vma=False)
```

```python
import math

import jax
import jax.numpy as jnp
import numpy as np
from jax import lax
from jax.sharding import Mesh
from jax.sharding import PartitionSpec as P

EPSILON = 1e-05
REQ = ("rz", "ry", "rc")


def layer_norm(values, gain, bias):
    center = values - jnp.mean(values, axis=-1, keepdims=True)
    spread = jnp.mean(center * center, axis=-1, keepdims=True)
    return center * lax.rsqrt(spread + EPSILON) * gain + bias


def split_req(mesh):
    column = mesh.devices[:, 0]
    try:
        cores = len({d.core_on_chip for d in column})
        ys = len({d.coords[1] for d in column})
        zs = len({d.coords[2] for d in column})
    except AttributeError:
        return (column.shape[0], 1, 1)
    if zs * ys * cores != column.shape[0]:
        return (column.shape[0], 1, 1)
    return (zs, ys, cores)


def gather_plane(block):
    return lax.all_gather(block, ("rz", "ry"), axis=0, tiled=False)


def swap_cores(plane):
    other = lax.ppermute(plane, "rc", [(0, 1), (1, 0)])
    mine = lax.axis_index("rc")
    cores = jnp.arange(2, dtype=jnp.int32).reshape(1, 2, 1, 1)
    whole = jnp.where(cores == mine, plane[:, None], other[:, None])
    return whole.reshape(-1, plane.shape[-1])


def local(
    owner_slab,
    segment_ids,
    head_weights,
    merge_weights,
    first_gain,
    first_bias,
    up_weights,
    down_weights,
    second_gain,
    second_bias,
    page_table,
    row_map,
):
    group = lax.axis_size("grp")
    owners = lax.axis_size(REQ)
    rows_all = owner_slab.shape[0]
    width = owner_slab.shape[1]
    quarter = rows_all // group
    local_heads = head_weights.shape[1]
    head_dim = head_weights.shape[2] // 3

    up_plane = gather_plane(up_weights)
    down_plane = gather_plane(jnp.transpose(down_weights))

    projected = jnp.einsum(
        "nd,dhc->nhc", owner_slab, head_weights, preferred_element_type=jnp.float32
    ).astype(jnp.bfloat16)
    queries = jnp.moveaxis(projected[:, :, :head_dim], 1, 0)
    key_rows = jnp.moveaxis(projected[:, :, head_dim : 2 * head_dim], 1, 0)
    value_rows = jnp.moveaxis(projected[:, :, 2 * head_dim :], 1, 0)
    segment = segment_ids[0]
    position = jnp.arange(rows_all, dtype=jnp.int32)
    allowed = (position[:, None] >= position[None, :]) & (segment[:, None] == segment[None, :])
    scale = 1.0 / math.sqrt(head_dim)

    def one_head(operands):
        query_head, key_head, value_head = operands
        scores = (
            lax.dot_general(
                query_head, key_head, (((1,), (1,)), ((), ())), preferred_element_type=jnp.float32
            )
            * scale
        )
        scores = jnp.where(allowed, scores, -1e30)
        probs = jax.nn.softmax(scores, axis=-1).astype(jnp.bfloat16)
        return jnp.dot(probs, value_head, preferred_element_type=jnp.float32).astype(jnp.bfloat16)

    attended = jnp.moveaxis(lax.map(one_head, (queries, key_rows, value_rows)), 0, 1)
    own = lax.axis_index("grp")
    own_rows = lax.dynamic_slice_in_dim(owner_slab, own * quarter, quarter, 0).astype(jnp.float32)
    partial_rows = jnp.einsum(
        "nhd,hde->ne", attended, merge_weights, preferred_element_type=jnp.float32
    )
    mixed = lax.psum_scatter(partial_rows, "grp", scatter_dimension=0, tiled=True)
    hidden = layer_norm(own_rows + mixed, first_gain, first_bias).astype(jnp.bfloat16)
    slots = quarter // owners
    placed = jnp.zeros_like(hidden).at[row_map[0, 0]].set(hidden)
    arrived = lax.all_to_all(
        placed.reshape(owners, slots, width), REQ, split_axis=0, concat_axis=0, tiled=True
    )
    even_rows = arrived.reshape(quarter, width)
    up_plane, down_plane, _ = lax.optimization_barrier((up_plane, down_plane, even_rows))
    up_full = swap_cores(up_plane)
    down_full_t = swap_cores(down_plane)
    copies = jnp.broadcast_to(even_rows[None], (group, quarter, width))
    group_rows = lax.all_to_all(copies, "grp", split_axis=0, concat_axis=0, tiled=True)
    group_rows = group_rows.reshape(group * quarter, width)
    raised = jnp.dot(group_rows, up_full, preferred_element_type=jnp.float32)
    activated = jax.nn.gelu(raised, approximate=False).astype(jnp.bfloat16)
    lowered_all = lax.dot_general(
        activated, down_full_t, (((1,), (1,)), ((), ())), preferred_element_type=jnp.float32
    )
    lowered = lax.psum_scatter(lowered_all, "grp", scatter_dimension=0, tiled=True)
    layer_out = layer_norm(
        even_rows.astype(jnp.float32) + lowered, second_gain, second_bias
    ).astype(jnp.bfloat16)
    page_count = page_table.shape[1]
    page_rows = rows_all // page_count
    stacked = projected[:, :, head_dim:].reshape(page_count, page_rows, local_heads, 2 * head_dim)
    cache_pages = jnp.zeros_like(stacked).at[page_table[0]].set(stacked)
    return (layer_out, cache_pages)


def solution(mesh):
    zs, ys, cores = split_req(mesh)
    devices = np.asarray(mesh.devices).reshape(zs, ys, cores, mesh.devices.shape[1])
    inner = Mesh(devices, REQ + ("grp",))
    in_specs = (
        P(REQ, None),
        P(REQ, None),
        P(None, "grp", None),
        P("grp", None, None),
        P(),
        P(),
        P(REQ, "grp"),
        P("grp", REQ),
        P(),
        P(),
        P(REQ, None),
        P(REQ, "grp", None),
    )
    out_specs = (P(REQ + ("grp",), None), P(REQ, None, "grp", None))
    return jax.shard_map(local, mesh=inner, in_specs=in_specs, out_specs=out_specs, check_vma=False)
```
